256 devices in a mesh: oi: 16 (over y, x_hi, core), oj: 16 (over z, x_lo).
Axes of the slice: x: 4 (x_hi: 2, x_lo: 2; x = x_hi * 2 + x_lo), y: 4, z: 8, core: 2. Of those that a mesh axis runs over, the one named last changes fastest.
Arguments:
- amps: bfloat16 [64, 64, 32768], P('oi', 'oj'), may hold values from -6 to 6
- ladder_w: bfloat16 [2016, 2016], P('oj'), may hold values from -0.125 to 0.125
- fock: bfloat16 [64, 64], replicated, may hold values from -0.75 to 0.75
- eps_occ: float32 [64], replicated, may hold values from -2 to -0.3
- eps_pair: float32 [32768], replicated, may hold values from 0.5 to 4
Outputs:
- update: bfloat16 [64, 64, 32768], P('oi', 'oj')
The draws below stay inside these ranges and needn't reach their ends.
All inputs are finite; a program needn't handle non-finite values.
Results may differ from the reference program's by a relative error of at most 0.0054.
Values may be sent and summed in bfloat16 or wider, within the bound.
No kernel may reach another device: no remote copies, remote signals or barrier semaphores. Data moves between devices by JAX's collectives and lax.ppermute only.
A program may use at most 128 MiB of HBM per device.

```python
import math
import jax
import jax.numpy as jnp
import numpy as np
from jax import lax

O = 64
NPAIR = 32768
PAIRS = 2016


def level_of(own_key, extent, cuts, low, largest):
    loudness = 1.0
    for axis_at, parts in cuts:
        steps = jax.random.uniform(jax.random.fold_in(jax.random.fold_in(own_key, 6), axis_at), (parts,), jnp.float32, low / len(cuts), largest / len(cuts))
        loudness = loudness * jnp.repeat(jnp.exp(steps), extent[axis_at] // parts).reshape((-1,) + (1,) * (len(extent) - 1 - axis_at))
    return loudness


def scatter_about(own_key, shape, scale, bound, cuts=(), kind=jnp.bfloat16):
    gain = level_of(own_key, shape, cuts, -0.22, 0.18) if cuts else 1.0
    array = jax.random.normal(own_key, shape, jnp.float32) * scale * gain
    return jnp.minimum(jnp.maximum(array, -bound), bound).astype(kind)


def setup_inputs(seed: int = 0) -> dict:
    arg_keys = jax.random.split(jax.random.key(seed), 6)
    return {
        "amps": scatter_about(arg_keys[0], (O, O, NPAIR), 1.0, 6.0, ((0, 16), (1, 16))),
        "ladder_w": scatter_about(arg_keys[1], (PAIRS, PAIRS), PAIRS ** -0.5, 0.125, ((0, 16),)),
        "fock": scatter_about(arg_keys[2], (O, O), O ** -0.5, 0.75),
        "eps_occ": jnp.clip(jax.random.uniform(arg_keys[3], (O,), jnp.float32, -2.0, -0.3), -2.0, -0.3),
        "eps_pair": jnp.clip(jax.random.uniform(arg_keys[4], (NPAIR,), jnp.float32, 0.5, 4.0), 0.5, 4.0),
    }


def pair_tables(occ):
    first, second = np.triu_indices(occ, 1)
    upper = (first * occ + second).astype(np.int32)
    lower = (second * occ + first).astype(np.int32)
    npairs = upper.shape[0]
    expand = np.full((occ * occ,), 2 * npairs, dtype=np.int32)
    expand[upper] = np.arange(npairs, dtype=np.int32)
    expand[lower] = npairs + np.arange(npairs, dtype=np.int32)
    return upper, lower, expand


def reference(amps, ladder_w, fock, eps_occ, eps_pair):
    upper, lower, expand = pair_tables(O)
    block = math.gcd(NPAIR, 4096)
    nblocks = NPAIR // block
    flat = amps.reshape(O * O, NPAIR)
    fock_wide = fock.astype(jnp.float32)

    def one_block(index):
        start = (index * block).astype(jnp.int32)
        cols = lax.dynamic_slice_in_dim(flat, start, block, 1)
        anti = (cols[upper].astype(jnp.float32) - cols[lower].astype(jnp.float32)).astype(jnp.bfloat16)
        ladder = jnp.dot(ladder_w.T, anti, preferred_element_type=jnp.float32)
        width = jnp.zeros((1, block), jnp.float32)
        full = jnp.concatenate([ladder, -ladder, width], axis=0)[expand].reshape(O, O, block)
        mixed = jnp.einsum("ikp,kj->ijp", cols.reshape(O, O, block).astype(jnp.float32), fock_wide)
        resid = (full - (mixed - jnp.transpose(mixed, (1, 0, 2)))).astype(jnp.bfloat16)
        resid = lax.optimization_barrier(resid)
        energies = lax.dynamic_slice_in_dim(eps_pair, start, block, 0)
        denom = energies[None, None, :] - eps_occ[:, None, None] - eps_occ[None, :, None]
        return (resid.astype(jnp.float32) / denom).astype(jnp.bfloat16)

    pieces = lax.map(one_block, jnp.arange(nblocks, dtype=jnp.int32))
    return jnp.transpose(pieces, (1, 2, 0, 3)).reshape(O, O, NPAIR)
```

```python
import jax
import jax.numpy as jnp
import numpy as np
from jax import lax
from jax.sharding import PartitionSpec as P


def pair_tables(occ):
    first, second = np.triu_indices(occ, 1)
    upper = (first * occ + second).astype(np.int32)
    lower = (second * occ + first).astype(np.int32)
    npairs = upper.shape[0]
    spread = np.full((occ * occ,), npairs, dtype=np.int32)
    spread[upper] = np.arange(npairs, dtype=np.int32)
    return (upper, lower, spread)


def on_device(amps, ladder_w, fock, eps_occ, eps_pair):
    rows_i, rows_j, total = amps.shape
    n_oi = lax.axis_size("oi")
    n_oj = lax.axis_size("oj")
    ndev = n_oi * n_oj
    width = total // ndev
    occ = rows_i * n_oi
    me_i = lax.axis_index("oi")
    me_j = lax.axis_index("oj")
    me = me_i * n_oj + me_j
    core = me_i % 2
    partner = [(a, a ^ 1) for a in range(n_oi)]

    send = amps.reshape(rows_i, rows_j, ndev, width).transpose(2, 0, 1, 3)
    recv = lax.all_to_all(send, ("oi", "oj"), 0, 0, tiled=True)
    pair_amps = (
        recv.reshape(n_oi, n_oj, rows_i, rows_j, width)
        .transpose(0, 2, 1, 3, 4)
        .reshape(occ, occ, width)
    )

    upper, lower, spread = pair_tables(occ)
    npairs = upper.shape[0]
    half = npairs // 2
    flat = pair_amps.reshape(occ * occ, width)
    anti = (flat[upper].astype(jnp.float32) - flat[lower].astype(jnp.float32)).astype(jnp.bfloat16)

    anti_other = lax.ppermute(anti, "oi", partner)
    w_part = lax.dynamic_slice_in_dim(ladder_w, core * half, half, 1)
    w_half = lax.all_gather(w_part, "oj", axis=0, tiled=True)
    both = jnp.concatenate([anti, anti_other], axis=1)
    contract = (((0,), (0,)), ((), ()))
    lad = lax.dot_general(w_half, both, contract, preferred_element_type=jnp.float32)
    lad_mine = lad[:, :width]
    lad_other = lax.ppermute(lad[:, width:], "oi", partner)
    first = jnp.where(core == 0, lad_mine, lad_other)
    second = jnp.where(core == 0, lad_other, lad_mine)
    ladder = jnp.concatenate([first, second, jnp.zeros((1, width), jnp.float32)], axis=0)

    upper_part = ladder[spread].reshape(occ, occ, width)
    mixed = jnp.einsum("ikp,kj->ijp", pair_amps, fock, preferred_element_type=jnp.float32)
    x = upper_part - mixed
    resid = x - jnp.transpose(x, (1, 0, 2))
    resid = lax.reduce_precision(resid, exponent_bits=8, mantissa_bits=7)
    energies = lax.dynamic_slice_in_dim(eps_pair, me * width, width, 0)
    denom = energies[None, None, :] - eps_occ[:, None, None] - eps_occ[None, :, None]
    upd = (resid / denom).astype(jnp.bfloat16)

    out_send = (
        upd.reshape(n_oi, rows_i, n_oj, rows_j, width)
        .transpose(0, 2, 1, 3, 4)
        .reshape(ndev, rows_i, rows_j, width)
    )
    out_recv = lax.all_to_all(out_send, ("oi", "oj"), 0, 0, tiled=True)
    return out_recv.transpose(1, 2, 0, 3).reshape(rows_i, rows_j, total)


def solution(mesh):
    in_specs = (P("oi", "oj", None), P("oj", None), P(), P(), P())
    out_specs = P("oi", "oj", None)
    return jax.shard_map(
        on_device, mesh=mesh, in_specs=in_specs, out_specs=out_specs, check_vma=False
    )
```

```python
import jax
import jax.numpy as jnp
import numpy as np
from jax import lax
from jax.sharding import PartitionSpec as P


def pair_tables(occ):
    first, second = np.triu_indices(occ, 1)
    upper = (first * occ + second).astype(np.int32)
    lower = (second * occ + first).astype(np.int32)
    npairs = upper.shape[0]
    spread = np.full((occ * occ,), npairs, dtype=np.int32)
    spread[upper] = np.arange(npairs, dtype=np.int32)
    return (upper, lower, spread)


FLIPS = (1, 4, 5)


def on_device(amps, ladder_w, fock, eps_occ, eps_pair):
    rows_i, rows_j, total = amps.shape
    n_oi = lax.axis_size("oi")
    n_oj = lax.axis_size("oj")
    ndev = n_oi * n_oj
    width = total // ndev
    occ = rows_i * n_oi
    me_i = lax.axis_index("oi")
    me_j = lax.axis_index("oj")
    me = me_i * n_oj + me_j
    q = ((me_i >> 2) & 1) * 2 + (me_i & 1)
    perms = [[(a, a ^ f) for a in range(n_oi)] for f in FLIPS]

    send = amps.reshape(rows_i, rows_j, ndev, width).transpose(2, 0, 1, 3)
    recv = lax.all_to_all(send, ("oi", "oj"), 0, 0, tiled=True)
    pair_amps = (
        recv.reshape(n_oi, n_oj, rows_i, rows_j, width)
        .transpose(0, 2, 1, 3, 4)
        .reshape(occ, occ, width)
    )

    upper, lower, spread = pair_tables(occ)
    npairs = upper.shape[0]
    part = npairs // 4
    flat = pair_amps.reshape(occ * occ, width)
    anti = (flat[upper].astype(jnp.float32) - flat[lower].astype(jnp.float32)).astype(jnp.bfloat16)

    anti_all = [anti] + [lax.ppermute(anti, "oi", p) for p in perms]
    w_part = lax.dynamic_slice_in_dim(ladder_w, q * part, part, 1)
    w_blocks = lax.all_gather(w_part, "oj", axis=0, tiled=False)
    both = jnp.concatenate(anti_all, axis=1).reshape(n_oj, npairs // n_oj, 4 * width)
    contract = (((0, 1), (0, 1)), ((), ()))
    lad = lax.dot_general(w_blocks, both, contract, preferred_element_type=jnp.float32)
    pieces = [lad[:, :width]] + [
        lax.ppermute(lad[:, (n + 1) * width : (n + 2) * width], "oi", p)
        for n, p in enumerate(perms)
    ]
    stack = jnp.stack(pieces)
    order = jnp.bitwise_xor(q, jnp.arange(4, dtype=q.dtype))
    ladder = jnp.take(stack, order, axis=0).reshape(npairs, width)
    ladder = jnp.concatenate([ladder, jnp.zeros((1, width), jnp.float32)], axis=0)

    upper_part = ladder[spread].reshape(occ, occ, width)
    mixed = jnp.einsum("ikp,kj->ijp", pair_amps, fock, preferred_element_type=jnp.float32)
    x = upper_part - mixed
    resid = x - jnp.transpose(x, (1, 0, 2))
    resid = lax.reduce_precision(resid, exponent_bits=8, mantissa_bits=7)
    energies = lax.dynamic_slice_in_dim(eps_pair, me * width, width, 0)
    denom = energies[None, None, :] - eps_occ[:, None, None] - eps_occ[None, :, None]
    upd = (resid / denom).astype(jnp.bfloat16)

    out_send = (
        upd.reshape(n_oi, rows_i, n_oj, rows_j, width)
        .transpose(0, 2, 1, 3, 4)
        .reshape(ndev, rows_i, rows_j, width)
    )
    out_recv = lax.all_to_all(out_send, ("oi", "oj"), 0, 0, tiled=True)
    return out_recv.transpose(1, 2, 0, 3).reshape(rows_i, rows_j, total)


def solution(mesh):
    in_specs = (P("oi", "oj", None), P("oj", None), P(), P(), P())
    out_specs = P("oi", "oj", None)
    return jax.shard_map(
        on_device, mesh=mesh, in_specs=in_specs, out_specs=out_specs, check_vma=False
    )
```

```python
import jax
import jax.numpy as jnp
import numpy as np
from jax import lax
from jax.sharding import PartitionSpec as P


def pair_tables(occ):
    first, second = np.triu_indices(occ, 1)
    upper = (first * occ + second).astype(np.int32)
    lower = (second * occ + first).astype(np.int32)
    npairs = upper.shape[0]
    spread = np.full((occ * occ,), npairs, dtype=np.int32)
    spread[upper] = np.arange(npairs, dtype=np.int32)
    return (upper, lower, spread)


FLIPS = (1, 4, 5)


def on_device(amps, ladder_w, fock, eps_occ, eps_pair):
    rows_i, rows_j, total = amps.shape
    n_oi = lax.axis_size("oi")
    n_oj = lax.axis_size("oj")
    ndev = n_oi * n_oj
    width = total // ndev
    occ = rows_i * n_oi
    me_i = lax.axis_index("oi")
    me_j = lax.axis_index("oj")
    me = me_i * n_oj + me_j
    q = ((me_i >> 2) & 1) * 2 + (me_i & 1)
    perms = [[(a, a ^ f) for a in range(n_oi)] for f in FLIPS]

    send = amps.reshape(rows_i, rows_j, ndev, width).transpose(2, 0, 1, 3)
    recv = lax.all_to_all(send, ("oi", "oj"), 0, 0, tiled=True)
    pair_amps = (
        recv.reshape(n_oi, n_oj, rows_i, rows_j, width)
        .transpose(0, 2, 1, 3, 4)
        .reshape(occ, occ, width)
    )

    upper, lower, spread = pair_tables(occ)
    npairs = upper.shape[0]
    part = npairs // 4
    flat = pair_amps.reshape(occ * occ, width)
    anti = (flat[upper].astype(jnp.float32) - flat[lower].astype(jnp.float32)).astype(jnp.bfloat16)

    from_core = lax.ppermute(anti, "oi", perms[0])
    from_y = lax.ppermute(anti, "oi", perms[1])
    from_diag = lax.ppermute(from_y, "oi", perms[0])
    anti_all = [anti, from_core, from_y, from_diag]
    w_part = lax.dynamic_slice_in_dim(ladder_w, q * part, part, 1)
    w_blocks = lax.all_gather(w_part, "oj", axis=0, tiled=False)
    both = jnp.concatenate(anti_all, axis=1).reshape(n_oj, npairs // n_oj, 4 * width)
    contract = (((0, 1), (0, 1)), ((), ()))
    lad = lax.dot_general(w_blocks, both, contract, preferred_element_type=jnp.float32)
    pieces = [lad[:, :width]] + [
        lax.ppermute(lad[:, (n + 1) * width : (n + 2) * width], "oi", p)
        for n, p in enumerate(perms)
    ]
    stack = jnp.stack(pieces)
    order = jnp.bitwise_xor(q, jnp.arange(4, dtype=q.dtype))
    ladder = jnp.take(stack, order, axis=0).reshape(npairs, width)
    ladder = jnp.concatenate([ladder, jnp.zeros((1, width), jnp.float32)], axis=0)

    upper_part = ladder[spread].reshape(occ, occ, width)
    mixed = jnp.einsum("ikp,kj->ijp", pair_amps, fock, preferred_element_type=jnp.float32)
    x = upper_part - mixed
    resid = x - jnp.transpose(x, (1, 0, 2))
    resid = lax.reduce_precision(resid, exponent_bits=8, mantissa_bits=7)
    energies = lax.dynamic_slice_in_dim(eps_pair, me * width, width, 0)
    denom = energies[None, None, :] - eps_occ[:, None, None] - eps_occ[None, :, None]
    upd = (resid / denom).astype(jnp.bfloat16)

    out_send = (
        upd.reshape(n_oi, rows_i, n_oj, rows_j, width)
        .transpose(0, 2, 1, 3, 4)
        .reshape(ndev, rows_i, rows_j, width)
    )
    out_recv = lax.all_to_all(out_send, ("oi", "oj"), 0, 0, tiled=True)
    return out_recv.transpose(1, 2, 0, 3).reshape(rows_i, rows_j, total)


def solution(mesh):
    in_specs = (P("oi", "oj", None), P("oj", None), P(), P(), P())
    out_specs = P("oi", "oj", None)
    return jax.shard_map(
        on_device, mesh=mesh, in_specs=in_specs, out_specs=out_specs, check_vma=False
    )
```

```python
import jax
import jax.numpy as jnp
import numpy as np
from jax import lax
from jax.experimental import pallas as pl
from jax.experimental.pallas import tpu as pltpu
from jax.sharding import PartitionSpec as P


def pair_tables(occ):
    first, second = np.triu_indices(occ, 1)
    upper = (first * occ + second).astype(np.int32)
    lower = (second * occ + first).astype(np.int32)
    npairs = upper.shape[0]
    spread = np.full((occ * occ,), npairs, dtype=np.int32)
    spread[upper] = np.arange(npairs, dtype=np.int32)
    return (upper, lower, spread)


FLIPS = (1, 4, 5)


def row_starts(occ):
    return [i * (occ - 1) - i * (i - 1) // 2 - i for i in range(occ)]


def anti_kernel(d_ref, o_ref, tmp_ref):
    occ = d_ref.shape[0]
    off = 0
    for k in range(occ - 1):
        n = occ - 1 - k
        tmp_ref[off : off + n, :] = d_ref[k, k + 1 : occ, :]
        off += n
    blocks, rows = o_ref.shape[0], o_ref.shape[1]
    for b in range(blocks):
        o_ref[b] = tmp_ref[b * rows : (b + 1) * rows, :].astype(o_ref.dtype)


def spread_kernel(q_ref, p0, p1, p2, p3, o_ref, lad_ref):
    pieces = (p0, p1, p2, p3)
    part = p0.shape[0]
    q = q_ref[0]
    lad_ref[0:8, :] = jnp.zeros((8, lad_ref.shape[1]), lad_ref.dtype)
    for r in range(4):
        for n in range(4):

            @pl.when(jnp.bitwise_xor(q, r) == n)
            def _():
                lad_ref[8 + r * part : 8 + (r + 1) * part, :] = pieces[n][...]

    occ, width = o_ref.shape[0], o_ref.shape[2]
    col = lax.broadcasted_iota(jnp.int32, (occ, width), 0)
    for i, s in enumerate(row_starts(occ)):
        o_ref[i] = jnp.where(col > i, lad_ref[7 + s : 7 + s + occ, :], 0.0)


def vmem_call(kernel, out_shape, scratch, *args, smem=0):
    spaces = [pltpu.SMEM] * smem + [pltpu.VMEM] * (len(args) - smem)
    return pl.pallas_call(
        kernel,
        out_shape=out_shape,
        in_specs=[pl.BlockSpec(memory_space=s) for s in spaces],
        out_specs=pl.BlockSpec(memory_space=pltpu.VMEM),
        scratch_shapes=scratch,
    )(*args)


def on_device(amps, ladder_w, fock, eps_occ, eps_pair):
    rows_i, rows_j, total = amps.shape
    n_oi = lax.axis_size("oi")
    n_oj = lax.axis_size("oj")
    ndev = n_oi * n_oj
    width = total // ndev
    occ = rows_i * n_oi
    me_i = lax.axis_index("oi")
    me_j = lax.axis_index("oj")
    me = me_i * n_oj + me_j
    q = ((me_i >> 2) & 1) * 2 + (me_i & 1)
    perms = [[(a, a ^ f) for a in range(n_oi)] for f in FLIPS]

    send = amps.reshape(rows_i, rows_j, ndev, width).transpose(2, 0, 1, 3)
    recv = lax.all_to_all(send, ("oi", "oj"), 0, 0, tiled=True)
    pair_amps = (
        recv.reshape(n_oi, n_oj, rows_i, rows_j, width)
        .transpose(0, 2, 1, 3, 4)
        .reshape(occ, occ, width)
    )

    upper, lower, spread = pair_tables(occ)
    npairs = upper.shape[0]
    part = npairs // 4
    swapped = jnp.transpose(pair_amps, (1, 0, 2))
    diff = pair_amps.astype(jnp.float32) - swapped.astype(jnp.float32)
    anti = vmem_call(
        anti_kernel,
        jax.ShapeDtypeStruct((n_oj, npairs // n_oj, width), jnp.bfloat16),
        [pltpu.VMEM((npairs, width), jnp.float32)],
        diff,
    )

    from_core = lax.ppermute(anti, "oi", perms[0])
    from_y = lax.ppermute(anti, "oi", perms[1])
    from_diag = lax.ppermute(from_y, "oi", perms[0])
    w_part = lax.dynamic_slice_in_dim(ladder_w, q * part, part, 1)
    w_blocks = lax.all_gather(w_part, "oj", axis=0, tiled=False)
    contract = (((0, 1), (0, 1)), ((), ()))

    def quarter(block):
        return lax.dot_general(w_blocks, block, contract, preferred_element_type=jnp.float32)

    own = quarter(anti)
    back = [
        lax.ppermute(quarter(block), "oi", p)
        for block, p in zip((from_core, from_y, from_diag), perms)
    ]
    upper_part = vmem_call(
        spread_kernel,
        jax.ShapeDtypeStruct((occ, occ, width), jnp.float32),
        [pltpu.VMEM((8 + npairs, width), jnp.float32)],
        q.astype(jnp.int32).reshape(1),
        own,
        *back,
        smem=1,
    )
    mixed = jnp.einsum("ikp,kj->ijp", pair_amps, fock, preferred_element_type=jnp.float32)
    x = upper_part - mixed
    resid = x - jnp.transpose(x, (1, 0, 2))
    resid = lax.reduce_precision(resid, exponent_bits=8, mantissa_bits=7)
    energies = lax.dynamic_slice_in_dim(eps_pair, me * width, width, 0)
    denom = energies[None, None, :] - eps_occ[:, None, None] - eps_occ[None, :, None]
    upd = (resid / denom).astype(jnp.bfloat16)

    out_send = (
        upd.reshape(n_oi, rows_i, n_oj, rows_j, width)
        .transpose(0, 2, 1, 3, 4)
        .reshape(ndev, rows_i, rows_j, width)
    )
    out_recv = lax.all_to_all(out_send, ("oi", "oj"), 0, 0, tiled=True)
    return out_recv.transpose(1, 2, 0, 3).reshape(rows_i, rows_j, total)


def solution(mesh):
    in_specs = (P("oi", "oj", None), P("oj", None), P(), P(), P())
    out_specs = P("oi", "oj", None)
    return jax.shard_map(
        on_device, mesh=mesh, in_specs=in_specs, out_specs=out_specs, check_vma=False
    )
```

```python
import jax
import jax.numpy as jnp
import numpy as np
from jax import lax
from jax.experimental import pallas as pl
from jax.experimental.pallas import tpu as pltpu
from jax.sharding import PartitionSpec as P


def pair_tables(occ):
    first, second = np.triu_indices(occ, 1)
    upper = (first * occ + second).astype(np.int32)
    lower = (second * occ + first).astype(np.int32)
    npairs = upper.shape[0]
    spread = np.full((occ * occ,), npairs, dtype=np.int32)
    spread[upper] = np.arange(npairs, dtype=np.int32)
    return (upper, lower, spread)


FLIPS = (1, 4, 5)


def row_starts(occ):
    return [i * (occ - 1) - i * (i - 1) // 2 - i for i in range(occ)]


def anti_kernel(d_ref, o_ref, tmp_ref):
    occ = d_ref.shape[0]
    off = 0
    for k in range(occ - 1):
        n = occ - 1 - k
        tmp_ref[off : off + n, :] = d_ref[k, k + 1 : occ, :]
        off += n
    blocks, rows = o_ref.shape[0], o_ref.shape[1]
    for b in range(blocks):
        o_ref[b] = tmp_ref[b * rows : (b + 1) * rows, :].astype(o_ref.dtype)


def spread_kernel(q_ref, p0, p1, p2, p3, o_ref, lad_ref):
    pieces = (p0, p1, p2, p3)
    part = p0.shape[0]
    q = q_ref[0]
    lad_ref[0:8, :] = jnp.zeros((8, lad_ref.shape[1]), lad_ref.dtype)
    for r in range(4):
        for n in range(4):

            @pl.when(jnp.bitwise_xor(q, r) == n)
            def _():
                lad_ref[8 + r * part : 8 + (r + 1) * part, :] = pieces[n][...]

    occ, width = o_ref.shape[0], o_ref.shape[2]
    col = lax.broadcasted_iota(jnp.int32, (occ, width), 0)
    for i, s in enumerate(row_starts(occ)):
        o_ref[i] = jnp.where(col > i, lad_ref[7 + s : 7 + s + occ, :], 0.0)


def vmem_call(kernel, out_shape, scratch, *args, smem=0):
    spaces = [pltpu.SMEM] * smem + [pltpu.VMEM] * (len(args) - smem)
    return pl.pallas_call(
        kernel,
        out_shape=out_shape,
        in_specs=[pl.BlockSpec(memory_space=s) for s in spaces],
        out_specs=pl.BlockSpec(memory_space=pltpu.VMEM),
        scratch_shapes=scratch,
    )(*args)


def on_device(amps, ladder_w, fock, eps_occ, eps_pair):
    rows_i, rows_j, total = amps.shape
    n_oi = lax.axis_size("oi")
    n_oj = lax.axis_size("oj")
    ndev = n_oi * n_oj
    width = total // ndev
    occ = rows_i * n_oi
    me_i = lax.axis_index("oi")
    me_j = lax.axis_index("oj")
    me = me_i * n_oj + me_j
    q = ((me_i >> 2) & 1) * 2 + (me_i & 1)
    perms = [[(a, a ^ f) for a in range(n_oi)] for f in FLIPS]

    send = amps.reshape(rows_i, rows_j, ndev, width).transpose(2, 0, 1, 3)
    recv = lax.all_to_all(send, ("oi", "oj"), 0, 0, tiled=True)
    pair_amps = (
        recv.reshape(n_oi, n_oj, rows_i, rows_j, width)
        .transpose(0, 2, 1, 3, 4)
        .reshape(occ, occ, width)
    )

    upper, lower, spread = pair_tables(occ)
    npairs = upper.shape[0]
    part = npairs // 4
    swapped = jnp.transpose(pair_amps, (1, 0, 2))
    diff = pair_amps.astype(jnp.float32) - swapped.astype(jnp.float32)
    anti = vmem_call(
        anti_kernel,
        jax.ShapeDtypeStruct((n_oj, npairs // n_oj, width), jnp.bfloat16),
        [pltpu.VMEM((npairs, width), jnp.float32)],
        diff,
    )

    halfb = n_oj // 2
    from_core = lax.ppermute(anti, "oi", perms[0])
    y_parts = [lax.ppermute(anti[s], "oi", perms[1]) for s in (slice(0, halfb), slice(halfb, None))]
    diag_parts = [lax.ppermute(v, "oi", perms[0]) for v in y_parts]
    w_part = lax.dynamic_slice_in_dim(ladder_w, q * part, part, 1)
    w_blocks = lax.all_gather(w_part, "oj", axis=0, tiled=False)
    contract = (((0, 1), (0, 1)), ((), ()))

    def quarter_of(w, block):
        return lax.dot_general(w, block, contract, preferred_element_type=jnp.float32)

    def quarter(block):
        return quarter_of(w_blocks, block)

    def quarter_split(parts):
        return quarter_of(w_blocks[:halfb], parts[0]) + quarter_of(w_blocks[halfb:], parts[1])

    def send_split(piece, p):
        rows = piece.shape[0] // 2
        moved = [lax.ppermute(piece[s], "oi", p) for s in (slice(0, rows), slice(rows, None))]
        return jnp.concatenate(moved, axis=0)

    own = quarter(anti)
    back = [
        lax.ppermute(quarter(from_core), "oi", perms[0]),
        send_split(quarter_split(y_parts), perms[1]),
        send_split(quarter_split(diag_parts), perms[2]),
    ]
    upper_part = vmem_call(
        spread_kernel,
        jax.ShapeDtypeStruct((occ, occ, width), jnp.float32),
        [pltpu.VMEM((8 + npairs, width), jnp.float32)],
        q.astype(jnp.int32).reshape(1),
        own,
        *back,
        smem=1,
    )
    mixed = jnp.einsum("ikp,kj->ijp", pair_amps, fock, preferred_element_type=jnp.float32)
    x = upper_part - mixed
    resid = x - jnp.transpose(x, (1, 0, 2))
    resid = lax.reduce_precision(resid, exponent_bits=8, mantissa_bits=7)
    energies = lax.dynamic_slice_in_dim(eps_pair, me * width, width, 0)
    denom = energies[None, None, :] - eps_occ[:, None, None] - eps_occ[None, :, None]
    upd = (resid / denom).astype(jnp.bfloat16)

    out_send = (
        upd.reshape(n_oi, rows_i, n_oj, rows_j, width)
        .transpose(0, 2, 1, 3, 4)
        .reshape(ndev, rows_i, rows_j, width)
    )
    out_recv = lax.all_to_all(out_send, ("oi", "oj"), 0, 0, tiled=True)
    return out_recv.transpose(1, 2, 0, 3).reshape(rows_i, rows_j, total)


def solution(mesh):
    in_specs = (P("oi", "oj", None), P("oj", None), P(), P(), P())
    out_specs = P("oi", "oj", None)
    return jax.shard_map(
        on_device, mesh=mesh, in_specs=in_specs, out_specs=out_specs, check_vma=False
    )
```

```python
import jax
import jax.numpy as jnp
import numpy as np
from jax import lax
from jax.experimental import pallas as pl
from jax.experimental.pallas import tpu as pltpu
from jax.sharding import PartitionSpec as P


def pair_tables(occ):
    first, second = np.triu_indices(occ, 1)
    upper = (first * occ + second).astype(np.int32)
    lower = (second * occ + first).astype(np.int32)
    npairs = upper.shape[0]
    spread = np.full((occ * occ,), npairs, dtype=np.int32)
    spread[upper] = np.arange(npairs, dtype=np.int32)
    return (upper, lower, spread)


FLIPS = (1, 4, 5)


def row_starts(occ):
    return [i * (occ - 1) - i * (i - 1) // 2 - i for i in range(occ)]


def anti_kernel(d_ref, o_ref, tmp_ref):
    occ = d_ref.shape[0]
    off = 0
    for k in range(occ - 1):
        n = occ - 1 - k
        tmp_ref[off : off + n, :] = d_ref[k, k + 1 : occ, :]
        off += n
    blocks, rows = o_ref.shape[0], o_ref.shape[1]
    for b in range(blocks):
        o_ref[b] = tmp_ref[b * rows : (b + 1) * rows, :].astype(o_ref.dtype)


def spread_kernel(q_ref, p0, p1, p2, p3, o_ref, lad_ref):
    pieces = (p0, p1, p2, p3)
    part = p0.shape[0]
    q = q_ref[0]
    lad_ref[0:8, :] = jnp.zeros((8, lad_ref.shape[1]), lad_ref.dtype)
    for r in range(4):
        for n in range(4):

            @pl.when(jnp.bitwise_xor(q, r) == n)
            def _():
                lad_ref[8 + r * part : 8 + (r + 1) * part, :] = pieces[n][...]

    occ, width = o_ref.shape[0], o_ref.shape[2]
    col = lax.broadcasted_iota(jnp.int32, (occ, width), 0)
    for i, s in enumerate(row_starts(occ)):
        o_ref[i] = jnp.where(col > i, lad_ref[7 + s : 7 + s + occ, :], 0.0)


def vmem_call(kernel, out_shape, scratch, *args, smem=0):
    spaces = [pltpu.SMEM] * smem + [pltpu.VMEM] * (len(args) - smem)
    return pl.pallas_call(
        kernel,
        out_shape=out_shape,
        in_specs=[pl.BlockSpec(memory_space=s) for s in spaces],
        out_specs=pl.BlockSpec(memory_space=pltpu.VMEM),
        scratch_shapes=scratch,
    )(*args)


def on_device(amps, ladder_w, fock, eps_occ, eps_pair):
    rows_i, rows_j, total = amps.shape
    n_oi = lax.axis_size("oi")
    n_oj = lax.axis_size("oj")
    ndev = n_oi * n_oj
    width = total // ndev
    occ = rows_i * n_oi
    me_i = lax.axis_index("oi")
    me_j = lax.axis_index("oj")
    me = me_i * n_oj + me_j
    q = ((me_i >> 2) & 1) * 2 + (me_i & 1)
    perms = [[(a, a ^ f) for a in range(n_oi)] for f in FLIPS]

    send = amps.reshape(rows_i, rows_j, ndev, width).transpose(2, 0, 1, 3)
    recv = lax.all_to_all(send, ("oi", "oj"), 0, 0, tiled=True)
    pair_amps = (
        recv.reshape(n_oi, n_oj, rows_i, rows_j, width)
        .transpose(0, 2, 1, 3, 4)
        .reshape(occ, occ, width)
    )

    upper, lower, spread = pair_tables(occ)
    npairs = upper.shape[0]
    part = npairs // 4
    swapped = jnp.transpose(pair_amps, (1, 0, 2))
    diff = pair_amps.astype(jnp.float32) - swapped.astype(jnp.float32)
    anti = vmem_call(
        anti_kernel,
        jax.ShapeDtypeStruct((n_oj, npairs // n_oj, width), jnp.bfloat16),
        [pltpu.VMEM((npairs, width), jnp.float32)],
        diff,
    )

    from_core = lax.ppermute(anti, "oi", perms[0])
    from_y = lax.ppermute(anti, "oi", perms[1])
    from_diag = lax.ppermute(from_y, "oi", perms[0])
    w_part = lax.dynamic_slice_in_dim(ladder_w, q * part, part, 1)
    shifted = [w_part] + [
        lax.ppermute(w_part, "oj", [(b, (b + s) % n_oj) for b in range(n_oj)])
        for s in range(1, n_oj)
    ]
    source = (me_j - jnp.arange(n_oj, dtype=me_j.dtype)) % n_oj
    w_blocks = jnp.zeros((n_oj,) + w_part.shape, w_part.dtype).at[source].set(jnp.stack(shifted))
    contract = (((0, 1), (0, 1)), ((), ()))

    def quarter(block):
        return lax.dot_general(w_blocks, block, contract, preferred_element_type=jnp.float32)

    own = quarter(anti)
    back = [
        lax.ppermute(quarter(block), "oi", p)
        for block, p in zip((from_core, from_y, from_diag), perms)
    ]
    upper_part = vmem_call(
        spread_kernel,
        jax.ShapeDtypeStruct((occ, occ, width), jnp.float32),
        [pltpu.VMEM((8 + npairs, width), jnp.float32)],
        q.astype(jnp.int32).reshape(1),
        own,
        *back,
        smem=1,
    )
    mixed = jnp.einsum("ikp,kj->ijp", pair_amps, fock, preferred_element_type=jnp.float32)
    x = upper_part - mixed
    resid = x - jnp.transpose(x, (1, 0, 2))
    resid = lax.reduce_precision(resid, exponent_bits=8, mantissa_bits=7)
    energies = lax.dynamic_slice_in_dim(eps_pair, me * width, width, 0)
    denom = energies[None, None, :] - eps_occ[:, None, None] - eps_occ[None, :, None]
    upd = (resid / denom).astype(jnp.bfloat16)

    out_send = (
        upd.reshape(n_oi, rows_i, n_oj, rows_j, width)
        .transpose(0, 2, 1, 3, 4)
        .reshape(ndev, rows_i, rows_j, width)
    )
    out_recv = lax.all_to_all(out_send, ("oi", "oj"), 0, 0, tiled=True)
    return out_recv.transpose(1, 2, 0, 3).reshape(rows_i, rows_j, total)


def solution(mesh):
    in_specs = (P("oi", "oj", None), P("oj", None), P(), P(), P())
    out_specs = P("oi", "oj", None)
    return jax.shard_map(
        on_device, mesh=mesh, in_specs=in_specs, out_specs=out_specs, check_vma=False
    )
```

```python
import jax
import jax.numpy as jnp
import numpy as np
from jax import lax
from jax.experimental import pallas as pl
from jax.experimental.pallas import tpu as pltpu
from jax.sharding import PartitionSpec as P


def pair_tables(occ):
    first, second = np.triu_indices(occ, 1)
    upper = (first * occ + second).astype(np.int32)
    lower = (second * occ + first).astype(np.int32)
    npairs = upper.shape[0]
    spread = np.full((occ * occ,), npairs, dtype=np.int32)
    spread[upper] = np.arange(npairs, dtype=np.int32)
    return (upper, lower, spread)


FLIPS = (1, 4, 5)


def row_starts(occ):
    return [i * (occ - 1) - i * (i - 1) // 2 - i for i in range(occ)]


def anti_kernel(d_ref, o_ref, tmp_ref):
    occ = d_ref.shape[0]
    off = 0
    for k in range(occ - 1):
        n = occ - 1 - k
        tmp_ref[off : off + n, :] = d_ref[k, k + 1 : occ, :]
        off += n
    blocks, rows = o_ref.shape[0], o_ref.shape[1]
    for b in range(blocks):
        o_ref[b] = tmp_ref[b * rows : (b + 1) * rows, :].astype(o_ref.dtype)


def spread_kernel(q_ref, a_ref, p0, p1, p2, p3, o_ref, lad_ref):
    pieces = (p0, p1, p2, p3)
    part = p0.shape[0]
    q = q_ref[0]
    lad_ref[0:8, :] = jnp.zeros((8, lad_ref.shape[1]), lad_ref.dtype)
    for r in range(4):
        for n in range(4):

            @pl.when(jnp.bitwise_xor(q, r) == n)
            def _():
                lad_ref[8 + r * part : 8 + (r + 1) * part, :] = pieces[n][...]

    occ, width = o_ref.shape[0], o_ref.shape[2]
    col = lax.broadcasted_iota(jnp.int32, (occ, width), 0)
    for i, s in enumerate(row_starts(occ)):
        o_ref[i] = jnp.where(col > i, lad_ref[7 + s : 7 + s + occ, :] - a_ref[i], 0.0)


def vmem_call(kernel, out_shape, scratch, *args, smem=0):
    spaces = [pltpu.SMEM] * smem + [pltpu.VMEM] * (len(args) - smem)
    return pl.pallas_call(
        kernel,
        out_shape=out_shape,
        in_specs=[pl.BlockSpec(memory_space=s) for s in spaces],
        out_specs=pl.BlockSpec(memory_space=pltpu.VMEM),
        scratch_shapes=scratch,
    )(*args)


def on_device(amps, ladder_w, fock, eps_occ, eps_pair):
    rows_i, rows_j, total = amps.shape
    n_oi = lax.axis_size("oi")
    n_oj = lax.axis_size("oj")
    ndev = n_oi * n_oj
    width = total // ndev
    occ = rows_i * n_oi
    me_i = lax.axis_index("oi")
    me_j = lax.axis_index("oj")
    me = me_i * n_oj + me_j
    q = ((me_i >> 2) & 1) * 2 + (me_i & 1)
    perms = [[(a, a ^ f) for a in range(n_oi)] for f in FLIPS]

    send = amps.reshape(rows_i, rows_j, ndev, width).transpose(2, 0, 1, 3)
    recv = lax.all_to_all(send, ("oi", "oj"), 0, 0, tiled=True)
    pair_amps = (
        recv.reshape(n_oi, n_oj, rows_i, rows_j, width)
        .transpose(0, 2, 1, 3, 4)
        .reshape(occ, occ, width)
    )

    upper, lower, spread = pair_tables(occ)
    npairs = upper.shape[0]
    part = npairs // 4
    swapped = jnp.transpose(pair_amps, (1, 0, 2))
    diff = pair_amps.astype(jnp.float32) - swapped.astype(jnp.float32)
    anti = vmem_call(
        anti_kernel,
        jax.ShapeDtypeStruct((n_oj, npairs // n_oj, width), jnp.bfloat16),
        [pltpu.VMEM((npairs, width), jnp.float32)],
        diff,
    )

    from_core = lax.ppermute(anti, "oi", perms[0])
    from_y = lax.ppermute(anti, "oi", perms[1])
    from_diag = lax.ppermute(from_y, "oi", perms[0])
    w_part = lax.dynamic_slice_in_dim(ladder_w, q * part, part, 1)
    w_blocks = lax.all_gather(w_part, "oj", axis=0, tiled=False)
    contract = (((0, 1), (0, 1)), ((), ()))

    def quarter(block):
        return lax.dot_general(w_blocks, block, contract, preferred_element_type=jnp.float32)

    mixed = jnp.einsum("ikp,kj->ijp", pair_amps, fock, preferred_element_type=jnp.float32)
    mixed_anti = mixed - jnp.transpose(mixed, (1, 0, 2))
    own = quarter(anti)
    back = [
        lax.ppermute(quarter(block), "oi", p)
        for block, p in zip((from_core, from_y, from_diag), perms)
    ]
    upper_part = vmem_call(
        spread_kernel,
        jax.ShapeDtypeStruct((occ, occ, width), jnp.float32),
        [pltpu.VMEM((8 + npairs, width), jnp.float32)],
        q.astype(jnp.int32).reshape(1),
        mixed_anti,
        own,
        *back,
        smem=1,
    )
    resid = upper_part - jnp.transpose(upper_part, (1, 0, 2))
    resid = lax.reduce_precision(resid, exponent_bits=8, mantissa_bits=7)
    energies = lax.dynamic_slice_in_dim(eps_pair, me * width, width, 0)
    denom = energies[None, None, :] - eps_occ[:, None, None] - eps_occ[None, :, None]
    upd = (resid / denom).astype(jnp.bfloat16)

    out_send = (
        upd.reshape(n_oi, rows_i, n_oj, rows_j, width)
        .transpose(0, 2, 1, 3, 4)
        .reshape(ndev, rows_i, rows_j, width)
    )
    out_recv = lax.all_to_all(out_send, ("oi", "oj"), 0, 0, tiled=True)
    return out_recv.transpose(1, 2, 0, 3).reshape(rows_i, rows_j, total)


def solution(mesh):
    in_specs = (P("oi", "oj", None), P("oj", None), P(), P(), P())
    out_specs = P("oi", "oj", None)
    return jax.shard_map(
        on_device, mesh=mesh, in_specs=in_specs, out_specs=out_specs, check_vma=False
    )
```

```python
import jax
import jax.numpy as jnp
import numpy as np
from jax import lax
from jax.experimental import pallas as pl
from jax.experimental.pallas import tpu as pltpu
from jax.sharding import PartitionSpec as P


def pair_tables(occ):
    first, second = np.triu_indices(occ, 1)
    upper = (first * occ + second).astype(np.int32)
    lower = (second * occ + first).astype(np.int32)
    npairs = upper.shape[0]
    spread = np.full((occ * occ,), npairs, dtype=np.int32)
    spread[upper] = np.arange(npairs, dtype=np.int32)
    return (upper, lower, spread)


FLIPS = (1, 4, 5)


def row_starts(occ):
    return [i * (occ - 1) - i * (i - 1) // 2 - i for i in range(occ)]


def anti_kernel(d_ref, o_ref, tmp_ref):
    occ = d_ref.shape[0]
    off = 0
    for k in range(occ - 1):
        n = occ - 1 - k
        tmp_ref[off : off + n, :] = d_ref[k, k + 1 : occ, :]
        off += n
    blocks, rows = o_ref.shape[0], o_ref.shape[1]
    for b in range(blocks):
        o_ref[b] = tmp_ref[b * rows : (b + 1) * rows, :].astype(o_ref.dtype)


def spread_kernel(q_ref, p0, p1, p2, p3, o_ref, lad_ref):
    pieces = (p0, p1, p2, p3)
    part = p0.shape[0]
    q = q_ref[0]
    lad_ref[0:8, :] = jnp.zeros((8, lad_ref.shape[1]), lad_ref.dtype)
    for r in range(4):
        for n in range(4):

            @pl.when(jnp.bitwise_xor(q, r) == n)
            def _():
                lad_ref[8 + r * part : 8 + (r + 1) * part, :] = pieces[n][...]

    occ, width = o_ref.shape[0], o_ref.shape[2]
    col = lax.broadcasted_iota(jnp.int32, (occ, width), 0)
    for i, s in enumerate(row_starts(occ)):
        o_ref[i] = jnp.where(col > i, lad_ref[7 + s : 7 + s + occ, :], 0.0)


def vmem_call(kernel, out_shape, scratch, *args, smem=0):
    spaces = [pltpu.SMEM] * smem + [pltpu.VMEM] * (len(args) - smem)
    return pl.pallas_call(
        kernel,
        out_shape=out_shape,
        in_specs=[pl.BlockSpec(memory_space=s) for s in spaces],
        out_specs=pl.BlockSpec(memory_space=pltpu.VMEM),
        scratch_shapes=scratch,
    )(*args)


def on_device(amps, ladder_w, fock, eps_occ, eps_pair):
    rows_i, rows_j, total = amps.shape
    n_oi = lax.axis_size("oi")
    n_oj = lax.axis_size("oj")
    ndev = n_oi * n_oj
    width = total // ndev
    occ = rows_i * n_oi
    me_i = lax.axis_index("oi")
    me_j = lax.axis_index("oj")
    me = me_i * n_oj + me_j
    q = ((me_i >> 2) & 1) * 2 + (me_i & 1)
    perms = [[(a, a ^ f) for a in range(n_oi)] for f in FLIPS]

    send = amps.reshape(rows_i, rows_j, ndev, width).transpose(2, 0, 1, 3)
    recv = lax.all_to_all(send, ("oi", "oj"), 0, 0, tiled=True)
    pair_amps = (
        recv.reshape(n_oi, n_oj, rows_i, rows_j, width)
        .transpose(0, 2, 1, 3, 4)
        .reshape(occ, occ, width)
    )

    upper, lower, spread = pair_tables(occ)
    npairs = upper.shape[0]
    part = npairs // 4
    swapped = jnp.transpose(pair_amps, (1, 0, 2))
    diff = pair_amps.astype(jnp.float32) - swapped.astype(jnp.float32)
    anti = vmem_call(
        anti_kernel,
        jax.ShapeDtypeStruct((n_oj, npairs // n_oj, width), jnp.bfloat16),
        [pltpu.VMEM((npairs, width), jnp.float32)],
        diff,
    )

    from_core = lax.ppermute(anti, "oi", perms[0])
    from_y = lax.ppermute(anti, "oi", perms[1])
    from_diag = lax.ppermute(from_y, "oi", perms[0])
    w_part = lax.dynamic_slice_in_dim(ladder_w, q * part, part, 1)
    w_blocks = lax.all_gather(w_part, "oj", axis=0, tiled=False)
    contract = (((0, 1), (0, 1)), ((), ()))

    def quarter(block):
        return lax.dot_general(w_blocks, block, contract, preferred_element_type=jnp.float32)

    own = quarter(anti)
    back = [lax.ppermute(quarter(from_core), "oi", perms[0])] + [
        lax.ppermute(quarter(block).astype(jnp.bfloat16), "oi", p).astype(jnp.float32)
        for block, p in zip((from_y, from_diag), perms[1:])
    ]
    upper_part = vmem_call(
        spread_kernel,
        jax.ShapeDtypeStruct((occ, occ, width), jnp.float32),
        [pltpu.VMEM((8 + npairs, width), jnp.float32)],
        q.astype(jnp.int32).reshape(1),
        own,
        *back,
        smem=1,
    )
    mixed = jnp.einsum("ikp,kj->ijp", pair_amps, fock, preferred_element_type=jnp.float32)
    x = upper_part - mixed
    resid = x - jnp.transpose(x, (1, 0, 2))
    resid = lax.reduce_precision(resid, exponent_bits=8, mantissa_bits=7)
    energies = lax.dynamic_slice_in_dim(eps_pair, me * width, width, 0)
    denom = energies[None, None, :] - eps_occ[:, None, None] - eps_occ[None, :, None]
    upd = (resid / denom).astype(jnp.bfloat16)

    out_send = (
        upd.reshape(n_oi, rows_i, n_oj, rows_j, width)
        .transpose(0, 2, 1, 3, 4)
        .reshape(ndev, rows_i, rows_j, width)
    )
    out_recv = lax.all_to_all(out_send, ("oi", "oj"), 0, 0, tiled=True)
    return out_recv.transpose(1, 2, 0, 3).reshape(rows_i, rows_j, total)


def solution(mesh):
    in_specs = (P("oi", "oj", None), P("oj", None), P(), P(), P())
    out_specs = P("oi", "oj", None)
    return jax.shard_map(
        on_device, mesh=mesh, in_specs=in_specs, out_specs=out_specs, check_vma=False
    )
```

```python
import jax
import jax.numpy as jnp
import numpy as np
from jax import lax
from jax.experimental import pallas as pl
from jax.experimental.pallas import tpu as pltpu
from jax.sharding import PartitionSpec as P


def pair_tables(occ):
    first, second = np.triu_indices(occ, 1)
    upper = (first * occ + second).astype(np.int32)
    lower = (second * occ + first).astype(np.int32)
    npairs = upper.shape[0]
    spread = np.full((occ * occ,), npairs, dtype=np.int32)
    spread[upper] = np.arange(npairs, dtype=np.int32)
    return (upper, lower, spread)


FLIPS = (1, 4, 5)


def row_starts(occ):
    return [i * (occ - 1) - i * (i - 1) // 2 - i for i in range(occ)]


def anti_kernel(d_ref, o_ref, tmp_ref):
    occ = d_ref.shape[0]
    off = 0
    for k in range(occ - 1):
        n = occ - 1 - k
        tmp_ref[off : off + n, :] = d_ref[k, k + 1 : occ, :]
        off += n
    blocks, rows = o_ref.shape[0], o_ref.shape[1]
    for b in range(blocks):
        o_ref[b] = tmp_ref[b * rows : (b + 1) * rows, :].astype(o_ref.dtype)


def spread_kernel(q_ref, p0, p1, p2, p3, o_ref, lad_ref):
    pieces = (p0, p1, p2, p3)
    part = p0.shape[0]
    q = q_ref[0]
    lad_ref[0:8, :] = jnp.zeros((8, lad_ref.shape[1]), lad_ref.dtype)
    for r in range(4):
        for n in range(4):

            @pl.when(jnp.bitwise_xor(q, r) == n)
            def _():
                lad_ref[8 + r * part : 8 + (r + 1) * part, :] = pieces[n][...].astype(lad_ref.dtype)

    occ, width = o_ref.shape[0], o_ref.shape[2]
    col = lax.broadcasted_iota(jnp.int32, (occ, width), 0)
    for i, s in enumerate(row_starts(occ)):
        o_ref[i] = jnp.where(col > i, lad_ref[7 + s : 7 + s + occ, :], 0.0)


def vmem_call(kernel, out_shape, scratch, *args, smem=0):
    spaces = [pltpu.SMEM] * smem + [pltpu.VMEM] * (len(args) - smem)
    return pl.pallas_call(
        kernel,
        out_shape=out_shape,
        in_specs=[pl.BlockSpec(memory_space=s) for s in spaces],
        out_specs=pl.BlockSpec(memory_space=pltpu.VMEM),
        scratch_shapes=scratch,
    )(*args)


def on_device(amps, ladder_w, fock, eps_occ, eps_pair):
    rows_i, rows_j, total = amps.shape
    n_oi = lax.axis_size("oi")
    n_oj = lax.axis_size("oj")
    ndev = n_oi * n_oj
    width = total // ndev
    occ = rows_i * n_oi
    me_i = lax.axis_index("oi")
    me_j = lax.axis_index("oj")
    me = me_i * n_oj + me_j
    q = ((me_i >> 2) & 1) * 2 + (me_i & 1)
    perms = [[(a, a ^ f) for a in range(n_oi)] for f in FLIPS]

    send = amps.reshape(rows_i, rows_j, ndev, width).transpose(2, 0, 1, 3)
    recv = lax.all_to_all(send, ("oi", "oj"), 0, 0, tiled=True)
    pair_amps = (
        recv.reshape(n_oi, n_oj, rows_i, rows_j, width)
        .transpose(0, 2, 1, 3, 4)
        .reshape(occ, occ, width)
    )

    upper, lower, spread = pair_tables(occ)
    npairs = upper.shape[0]
    part = npairs // 4
    swapped = jnp.transpose(pair_amps, (1, 0, 2))
    diff = pair_amps.astype(jnp.float32) - swapped.astype(jnp.float32)
    anti = vmem_call(
        anti_kernel,
        jax.ShapeDtypeStruct((n_oj, npairs // n_oj, width), jnp.bfloat16),
        [pltpu.VMEM((npairs, width), jnp.float32)],
        diff,
    )

    from_core = lax.ppermute(anti, "oi", perms[0])
    from_y = lax.ppermute(anti, "oi", perms[1])
    from_diag = lax.ppermute(from_y, "oi", perms[0])
    w_part = lax.dynamic_slice_in_dim(ladder_w, q * part, part, 1)
    w_blocks = lax.all_gather(w_part, "oj", axis=0, tiled=False)
    contract = (((0, 1), (0, 1)), ((), ()))

    def quarter(block):
        return lax.dot_general(w_blocks, block, contract, preferred_element_type=jnp.float32)

    own = quarter(anti)
    back = [lax.ppermute(quarter(from_core), "oi", perms[0])] + [
        lax.ppermute(quarter(block).astype(jnp.bfloat16), "oi", p)
        for block, p in zip((from_y, from_diag), perms[1:])
    ]
    upper_part = vmem_call(
        spread_kernel,
        jax.ShapeDtypeStruct((occ, occ, width), jnp.float32),
        [pltpu.VMEM((8 + npairs, width), jnp.float32)],
        q.astype(jnp.int32).reshape(1),
        own,
        *back,
        smem=1,
    )
    mixed = jnp.einsum("ikp,kj->ijp", pair_amps, fock, preferred_element_type=jnp.float32)
    x = upper_part - mixed
    resid = x - jnp.transpose(x, (1, 0, 2))
    resid = lax.reduce_precision(resid, exponent_bits=8, mantissa_bits=7)
    energies = lax.dynamic_slice_in_dim(eps_pair, me * width, width, 0)
    denom = energies[None, None, :] - eps_occ[:, None, None] - eps_occ[None, :, None]
    upd = (resid / denom).astype(jnp.bfloat16)

    out_send = (
        upd.reshape(n_oi, rows_i, n_oj, rows_j, width)
        .transpose(0, 2, 1, 3, 4)
        .reshape(ndev, rows_i, rows_j, width)
    )
    out_recv = lax.all_to_all(out_send, ("oi", "oj"), 0, 0, tiled=True)
    return out_recv.transpose(1, 2, 0, 3).reshape(rows_i, rows_j, total)


def solution(mesh):
    in_specs = (P("oi", "oj", None), P("oj", None), P(), P(), P())
    out_specs = P("oi", "oj", None)
    return jax.shard_map(
        on_device, mesh=mesh, in_specs=in_specs, out_specs=out_specs, check_vma=False
    )
```

```python
import jax
import jax.numpy as jnp
import numpy as np
from jax import lax
from jax.experimental import pallas as pl
from jax.experimental.pallas import tpu as pltpu
from jax.sharding import PartitionSpec as P


def pair_tables(occ):
    first, second = np.triu_indices(occ, 1)
    upper = (first * occ + second).astype(np.int32)
    lower = (second * occ + first).astype(np.int32)
    npairs = upper.shape[0]
    spread = np.full((occ * occ,), npairs, dtype=np.int32)
    spread[upper] = np.arange(npairs, dtype=np.int32)
    return (upper, lower, spread)


FLIPS = (1, 4, 5)


def row_starts(occ):
    return [i * (occ - 1) - i * (i - 1) // 2 - i for i in range(occ)]


def anti_kernel(d_ref, o_ref, tmp_ref):
    occ = d_ref.shape[0]
    off = 0
    for k in range(occ - 1):
        n = occ - 1 - k
        tmp_ref[off : off + n, :] = d_ref[k, k + 1 : occ, :]
        off += n
    blocks, rows = o_ref.shape[0], o_ref.shape[1]
    for b in range(blocks):
        o_ref[b] = tmp_ref[b * rows : (b + 1) * rows, :].astype(o_ref.dtype)


def spread_kernel(q_ref, p0, p1, p2, p3, o_ref, lad_ref):
    pieces = (p0, p1, p2, p3)
    part = p0.shape[0]
    q = q_ref[0]
    lad_ref[0:8, :] = jnp.zeros((8, lad_ref.shape[1]), lad_ref.dtype)
    for r in range(4):
        for n in range(4):

            @pl.when(jnp.bitwise_xor(q, r) == n)
            def _():
                lad_ref[8 + r * part : 8 + (r + 1) * part, :] = pieces[n][...].astype(lad_ref.dtype)

    occ, width = o_ref.shape[0], o_ref.shape[2]
    col = lax.broadcasted_iota(jnp.int32, (occ, width), 0)
    for i, s in enumerate(row_starts(occ)):
        o_ref[i] = jnp.where(col > i, lad_ref[7 + s : 7 + s + occ, :], 0.0)


def vmem_call(kernel, out_shape, scratch, *args, smem=0):
    spaces = [pltpu.SMEM] * smem + [pltpu.VMEM] * (len(args) - smem)
    return pl.pallas_call(
        kernel,
        out_shape=out_shape,
        in_specs=[pl.BlockSpec(memory_space=s) for s in spaces],
        out_specs=pl.BlockSpec(memory_space=pltpu.VMEM),
        scratch_shapes=scratch,
    )(*args)


def on_device(amps, ladder_w, fock, eps_occ, eps_pair):
    rows_i, rows_j, total = amps.shape
    n_oi = lax.axis_size("oi")
    n_oj = lax.axis_size("oj")
    ndev = n_oi * n_oj
    width = total // ndev
    occ = rows_i * n_oi
    me_i = lax.axis_index("oi")
    me_j = lax.axis_index("oj")
    me = me_i * n_oj + me_j
    q = ((me_i >> 2) & 1) * 2 + (me_i & 1)
    perms = [[(a, a ^ f) for a in range(n_oi)] for f in FLIPS]

    send = amps.reshape(rows_i, rows_j, ndev, width)
    recv = lax.all_to_all(send, ("oi", "oj"), 2, 2, tiled=True)
    pair_amps = (
        recv.reshape(rows_i, rows_j, n_oi, n_oj, width)
        .transpose(2, 0, 3, 1, 4)
        .reshape(occ, occ, width)
    )

    upper, lower, spread = pair_tables(occ)
    npairs = upper.shape[0]
    part = npairs // 4
    swapped = jnp.transpose(pair_amps, (1, 0, 2))
    diff = pair_amps.astype(jnp.float32) - swapped.astype(jnp.float32)
    anti = vmem_call(
        anti_kernel,
        jax.ShapeDtypeStruct((n_oj, npairs // n_oj, width), jnp.bfloat16),
        [pltpu.VMEM((npairs, width), jnp.float32)],
        diff,
    )

    from_core = lax.ppermute(anti, "oi", perms[0])
    from_y = lax.ppermute(anti, "oi", perms[1])
    from_diag = lax.ppermute(from_y, "oi", perms[0])
    w_part = lax.dynamic_slice_in_dim(ladder_w, q * part, part, 1)
    w_blocks = lax.all_gather(w_part, "oj", axis=0, tiled=False)
    contract = (((0, 1), (0, 1)), ((), ()))

    def quarter(block):
        return lax.dot_general(w_blocks, block, contract, preferred_element_type=jnp.float32)

    own = quarter(anti)
    back = [lax.ppermute(quarter(from_core), "oi", perms[0])] + [
        lax.ppermute(quarter(block).astype(jnp.bfloat16), "oi", p)
        for block, p in zip((from_y, from_diag), perms[1:])
    ]
    upper_part = vmem_call(
        spread_kernel,
        jax.ShapeDtypeStruct((occ, occ, width), jnp.float32),
        [pltpu.VMEM((8 + npairs, width), jnp.float32)],
        q.astype(jnp.int32).reshape(1),
        own,
        *back,
        smem=1,
    )
    mixed = jnp.einsum("ikp,kj->ijp", pair_amps, fock, preferred_element_type=jnp.float32)
    x = upper_part - mixed
    resid = x - jnp.transpose(x, (1, 0, 2))
    resid = lax.reduce_precision(resid, exponent_bits=8, mantissa_bits=7)
    energies = lax.dynamic_slice_in_dim(eps_pair, me * width, width, 0)
    denom = energies[None, None, :] - eps_occ[:, None, None] - eps_occ[None, :, None]
    upd = (resid / denom).astype(jnp.bfloat16)

    out_send = (
        upd.reshape(n_oi, rows_i, n_oj, rows_j, width)
        .transpose(0, 2, 1, 3, 4)
        .reshape(ndev, rows_i, rows_j, width)
    )
    out_recv = lax.all_to_all(out_send, ("oi", "oj"), 0, 0, tiled=True)
    return out_recv.transpose(1, 2, 0, 3).reshape(rows_i, rows_j, total)


def solution(mesh):
    in_specs = (P("oi", "oj", None), P("oj", None), P(), P(), P())
    out_specs = P("oi", "oj", None)
    return jax.shard_map(
        on_device, mesh=mesh, in_specs=in_specs, out_specs=out_specs, check_vma=False
    )
```

```python
import jax
import jax.numpy as jnp
import numpy as np
from jax import lax
from jax.experimental import pallas as pl
from jax.experimental.pallas import tpu as pltpu
from jax.sharding import PartitionSpec as P


def pair_tables(occ):
    first, second = np.triu_indices(occ, 1)
    upper = (first * occ + second).astype(np.int32)
    lower = (second * occ + first).astype(np.int32)
    npairs = upper.shape[0]
    spread = np.full((occ * occ,), npairs, dtype=np.int32)
    spread[upper] = np.arange(npairs, dtype=np.int32)
    return (upper, lower, spread)


FLIPS = (1, 4, 5)


def row_starts(occ):
    return [i * (occ - 1) - i * (i - 1) // 2 - i for i in range(occ)]


def anti_kernel(d_ref, o_ref, tmp_ref):
    occ = d_ref.shape[0]
    off = 0
    for k in range(occ - 1):
        n = occ - 1 - k
        tmp_ref[off : off + n, :] = d_ref[k, k + 1 : occ, :]
        off += n
    blocks, rows = o_ref.shape[0], o_ref.shape[1]
    for b in range(blocks):
        o_ref[b] = tmp_ref[b * rows : (b + 1) * rows, :].astype(o_ref.dtype)


def spread_kernel(q_ref, *refs):
    o_ref, lad_ref = refs[-2], refs[-1]
    halves = refs[:-2]
    rows = halves[0].shape[0]
    q = q_ref[0]
    lad_ref[0:8, :] = jnp.zeros((8, lad_ref.shape[1]), lad_ref.dtype)
    for r in range(4):
        for n in range(4):

            @pl.when(jnp.bitwise_xor(q, r) == n)
            def _():
                for h in range(2):
                    start = 8 + (2 * r + h) * rows
                    lad_ref[start : start + rows, :] = halves[2 * n + h][...].astype(lad_ref.dtype)

    occ, width = o_ref.shape[0], o_ref.shape[2]
    col = lax.broadcasted_iota(jnp.int32, (occ, width), 0)
    for i, s in enumerate(row_starts(occ)):
        o_ref[i] = jnp.where(col > i, lad_ref[7 + s : 7 + s + occ, :], 0.0)


def vmem_call(kernel, out_shape, scratch, *args, smem=0):
    spaces = [pltpu.SMEM] * smem + [pltpu.VMEM] * (len(args) - smem)
    return pl.pallas_call(
        kernel,
        out_shape=out_shape,
        in_specs=[pl.BlockSpec(memory_space=s) for s in spaces],
        out_specs=pl.BlockSpec(memory_space=pltpu.VMEM),
        scratch_shapes=scratch,
    )(*args)


def on_device(amps, ladder_w, fock, eps_occ, eps_pair):
    rows_i, rows_j, total = amps.shape
    n_oi = lax.axis_size("oi")
    n_oj = lax.axis_size("oj")
    ndev = n_oi * n_oj
    width = total // ndev
    occ = rows_i * n_oi
    me_i = lax.axis_index("oi")
    me_j = lax.axis_index("oj")
    me = me_i * n_oj + me_j
    q = ((me_i >> 2) & 1) * 2 + (me_i & 1)
    perms = [[(a, a ^ f) for a in range(n_oi)] for f in FLIPS]

    send = amps.reshape(rows_i, rows_j, ndev, width).transpose(2, 0, 1, 3)
    recv = lax.all_to_all(send, ("oi", "oj"), 0, 0, tiled=True)
    pair_amps = (
        recv.reshape(n_oi, n_oj, rows_i, rows_j, width)
        .transpose(0, 2, 1, 3, 4)
        .reshape(occ, occ, width)
    )

    upper, lower, spread = pair_tables(occ)
    npairs = upper.shape[0]
    part = npairs // 4
    swapped = jnp.transpose(pair_amps, (1, 0, 2))
    diff = pair_amps.astype(jnp.float32) - swapped.astype(jnp.float32)
    anti = vmem_call(
        anti_kernel,
        jax.ShapeDtypeStruct((n_oj, npairs // n_oj, width), jnp.bfloat16),
        [pltpu.VMEM((npairs, width), jnp.float32)],
        diff,
    )

    from_core = lax.ppermute(anti, "oi", perms[0])
    from_y = lax.ppermute(anti, "oi", perms[1])
    from_diag = lax.ppermute(from_y, "oi", perms[0])
    half = part // 2
    w_halves = [
        lax.all_gather(
            lax.dynamic_slice_in_dim(ladder_w, q * part + h * half, half, 1), "oj", axis=0, tiled=False
        )
        for h in range(2)
    ]
    contract = (((0, 1), (0, 1)), ((), ()))

    def quarter(w, block):
        return lax.dot_general(w, block, contract, preferred_element_type=jnp.float32)

    pieces = []
    for n, block in enumerate((anti, from_core, from_y, from_diag)):
        for w in w_halves:
            v = quarter(w, block)
            if n >= 2:
                v = v.astype(jnp.bfloat16)
            if n >= 1:
                v = lax.ppermute(v, "oi", perms[n - 1])
            pieces.append(v)
    upper_part = vmem_call(
        spread_kernel,
        jax.ShapeDtypeStruct((occ, occ, width), jnp.float32),
        [pltpu.VMEM((8 + npairs, width), jnp.float32)],
        q.astype(jnp.int32).reshape(1),
        *pieces,
        smem=1,
    )
    mixed = jnp.einsum("ikp,kj->ijp", pair_amps, fock, preferred_element_type=jnp.float32)
    x = upper_part - mixed
    resid = x - jnp.transpose(x, (1, 0, 2))
    resid = lax.reduce_precision(resid, exponent_bits=8, mantissa_bits=7)
    energies = lax.dynamic_slice_in_dim(eps_pair, me * width, width, 0)
    denom = energies[None, None, :] - eps_occ[:, None, None] - eps_occ[None, :, None]
    upd = (resid / denom).astype(jnp.bfloat16)

    out_send = (
        upd.reshape(n_oi, rows_i, n_oj, rows_j, width)
        .transpose(0, 2, 1, 3, 4)
        .reshape(ndev, rows_i, rows_j, width)
    )
    out_recv = lax.all_to_all(out_send, ("oi", "oj"), 0, 0, tiled=True)
    return out_recv.transpose(1, 2, 0, 3).reshape(rows_i, rows_j, total)


def solution(mesh):
    in_specs = (P("oi", "oj", None), P("oj", None), P(), P(), P())
    out_specs = P("oi", "oj", None)
    return jax.shard_map(
        on_device, mesh=mesh, in_specs=in_specs, out_specs=out_specs, check_vma=False
    )
```

```python
import jax
import jax.numpy as jnp
import numpy as np
from jax import lax
from jax.experimental import pallas as pl
from jax.experimental.pallas import tpu as pltpu
from jax.sharding import PartitionSpec as P


def pair_tables(occ):
    first, second = np.triu_indices(occ, 1)
    upper = (first * occ + second).astype(np.int32)
    lower = (second * occ + first).astype(np.int32)
    npairs = upper.shape[0]
    spread = np.full((occ * occ,), npairs, dtype=np.int32)
    spread[upper] = np.arange(npairs, dtype=np.int32)
    return (upper, lower, spread)


FLIPS = (1, 4, 5)


def row_starts(occ):
    return [i * (occ - 1) - i * (i - 1) // 2 - i for i in range(occ)]


def anti_kernel(d_ref, o_ref, tmp_ref):
    occ = d_ref.shape[0]
    off = 0
    for k in range(occ - 1):
        n = occ - 1 - k
        tmp_ref[off : off + n, :] = d_ref[k, k + 1 : occ, :]
        off += n
    blocks, rows = o_ref.shape[0], o_ref.shape[1]
    for b in range(blocks):
        o_ref[b] = tmp_ref[b * rows : (b + 1) * rows, :].astype(o_ref.dtype)


def spread_kernel(q_ref, p0, p1, p2, p3, o_ref, lad_ref):
    pieces = (p0, p1, p2, p3)
    part = p0.shape[0]
    q = q_ref[0]
    lad_ref[0:8, :] = jnp.zeros((8, lad_ref.shape[1]), lad_ref.dtype)
    for r in range(4):
        for n in range(4):

            @pl.when(jnp.bitwise_xor(q, r) == n)
            def _():
                lad_ref[8 + r * part : 8 + (r + 1) * part, :] = pieces[n][...].astype(lad_ref.dtype)

    occ, width = o_ref.shape[0], o_ref.shape[2]
    col = lax.broadcasted_iota(jnp.int32, (occ, width), 0)
    for i, s in enumerate(row_starts(occ)):
        o_ref[i] = jnp.where(col > i, lad_ref[7 + s : 7 + s + occ, :], 0.0)


def vmem_call(kernel, out_shape, scratch, *args, smem=0):
    spaces = [pltpu.SMEM] * smem + [pltpu.VMEM] * (len(args) - smem)
    return pl.pallas_call(
        kernel,
        out_shape=out_shape,
        in_specs=[pl.BlockSpec(memory_space=s) for s in spaces],
        out_specs=pl.BlockSpec(memory_space=pltpu.VMEM),
        scratch_shapes=scratch,
    )(*args)


def on_device(amps, ladder_w, fock, eps_occ, eps_pair):
    rows_i, rows_j, total = amps.shape
    n_oi = lax.axis_size("oi")
    n_oj = lax.axis_size("oj")
    ndev = n_oi * n_oj
    width = total // ndev
    occ = rows_i * n_oi
    me_i = lax.axis_index("oi")
    me_j = lax.axis_index("oj")
    me = me_i * n_oj + me_j
    q = ((me_i >> 2) & 1) * 2 + (me_i & 1)
    perms = [[(a, a ^ f) for a in range(n_oi)] for f in FLIPS]

    send = amps.reshape(rows_i, rows_j, ndev, width).transpose(2, 0, 1, 3)
    recv = lax.all_to_all(send, ("oi", "oj"), 0, 0, tiled=True)
    pair_amps = (
        recv.reshape(n_oi, n_oj, rows_i, rows_j, width)
        .transpose(0, 2, 1, 3, 4)
        .reshape(occ, occ, width)
    )

    upper, lower, spread = pair_tables(occ)
    npairs = upper.shape[0]
    part = npairs // 4
    swapped = jnp.transpose(pair_amps, (1, 0, 2))
    diff = pair_amps.astype(jnp.float32) - swapped.astype(jnp.float32)
    anti = vmem_call(
        anti_kernel,
        jax.ShapeDtypeStruct((n_oj, npairs // n_oj, width), jnp.bfloat16),
        [pltpu.VMEM((npairs, width), jnp.float32)],
        diff,
    )

    from_core = lax.ppermute(anti, "oi", perms[0])
    from_y = lax.ppermute(anti, "oi", perms[1])
    from_diag = lax.ppermute(from_y, "oi", perms[0])
    w_part = lax.dynamic_slice_in_dim(ladder_w, q * part, part, 1)
    w_blocks = lax.all_gather(w_part, "oj", axis=0, tiled=False)
    contract = (((0, 1), (0, 1)), ((), ()))

    def quarter(block):
        return lax.dot_general(w_blocks, block, contract, preferred_element_type=jnp.float32)

    far = quarter(jnp.concatenate([from_y, from_diag], axis=2)).astype(jnp.bfloat16)
    far_back = [
        lax.ppermute(far[:, n * width : (n + 1) * width], "oi", p)
        for n, p in enumerate(perms[1:])
    ]
    own = quarter(anti)
    back = [lax.ppermute(quarter(from_core), "oi", perms[0])] + far_back
    upper_part = vmem_call(
        spread_kernel,
        jax.ShapeDtypeStruct((occ, occ, width), jnp.float32),
        [pltpu.VMEM((8 + npairs, width), jnp.float32)],
        q.astype(jnp.int32).reshape(1),
        own,
        *back,
        smem=1,
    )
    mixed = jnp.einsum("ikp,kj->ijp", pair_amps, fock, preferred_element_type=jnp.float32)
    x = upper_part - mixed
    resid = x - jnp.transpose(x, (1, 0, 2))
    resid = lax.reduce_precision(resid, exponent_bits=8, mantissa_bits=7)
    energies = lax.dynamic_slice_in_dim(eps_pair, me * width, width, 0)
    denom = energies[None, None, :] - eps_occ[:, None, None] - eps_occ[None, :, None]
    upd = (resid / denom).astype(jnp.bfloat16)

    out_send = (
        upd.reshape(n_oi, rows_i, n_oj, rows_j, width)
        .transpose(0, 2, 1, 3, 4)
        .reshape(ndev, rows_i, rows_j, width)
    )
    out_recv = lax.all_to_all(out_send, ("oi", "oj"), 0, 0, tiled=True)
    return out_recv.transpose(1, 2, 0, 3).reshape(rows_i, rows_j, total)


def solution(mesh):
    in_specs = (P("oi", "oj", None), P("oj", None), P(), P(), P())
    out_specs = P("oi", "oj", None)
    return jax.shard_map(
        on_device, mesh=mesh, in_specs=in_specs, out_specs=out_specs, check_vma=False
    )
```
